128 devices in a mesh: member: 8 (over x_hi, z), dp: 16 (over x_lo, y, core).
Axes of the slice: x: 4 (x_hi: 2, x_lo: 2; x = x_hi * 2 + x_lo), y: 4, z: 4, core: 2. Of those that a mesh axis runs over, the one named last changes fastest.
Arguments:
- latents: bfloat16 [8, 64, 16, 16, 640], P('member', 'dp'), may hold values from -6 to 6
- cotangent: bfloat16 [8, 64, 16, 16, 640], P('member', 'dp'), may hold values from -6 to 6
- weights: float32 [8, 640, 5760], P('member', 'dp'), may hold values from -6 to 6
- first_moment: float32 [8, 640, 5760], P('member', 'dp'), may hold values from -1.2 to 1.2
- second_moment: float32 [8, 640, 5760], P('member', 'dp'), may hold values from 0.02 to 0.5
- sources: int32 [8], replicated, may hold values from 0 to 7, as said below
Outputs:
- latent_grad: bfloat16 [8, 64, 16, 16, 640], P('member', 'dp')
- new_weights: float32 [8, 640, 5760], P('member', 'dp')
- new_first: float32 [8, 640, 5760], P('member', 'dp')
- new_second: float32 [8, 640, 5760], P('member', 'dp')
The draws below stay inside these ranges and needn't reach their ends.
Inputs may be any that keep to these rules, and one draw needn't show every extreme that they name: sources[k] = k for every member that takes no copy; a member that takes a copy names a member that names itself; at most one quarter of the members (at least one) take copies, and at most one quarter (at least one) are named by others.
All inputs are finite; a program needn't handle non-finite values.
Results may differ from the reference program's by a relative error of at most 0.006.
Values may be sent and summed in bfloat16 or wider, within the bound.
No kernel may reach another device: no remote copies, remote signals or barrier semaphores. Data moves between devices by JAX's collectives and lax.ppermute only.
A program may use at most 128 MiB of HBM per device.

```python
import math
import jax
import jax.numpy as jnp
from jax import lax

CH_IN = 640
CH_OUT = 640
CROP = 16
IMG_DEV = 4
ADAM_STEP = 10
MEMBERS = 8
BATCH = 64
N_DP = 16


def draw_sources(key, part):
    rank_of = jax.random.permutation(jax.random.fold_in(key, 7), MEMBERS)
    by_rank = jnp.argsort(rank_of, stable=True)
    quarter = max(MEMBERS // 4, 1)
    chosen = jax.random.randint(jax.random.fold_in(key, 11), (MEMBERS,), 0, quarter)
    losing = rank_of >= MEMBERS - quarter
    return jnp.where(losing, by_rank[chosen], jnp.arange(MEMBERS)).astype(jnp.int32)


def levels(stream_key, extent, split, least, high):
    level = 1.0
    for axis_at, shards_of in split:
        steps = jax.random.uniform(jax.random.fold_in(jax.random.fold_in(stream_key, 6), axis_at), (shards_of,), jnp.float32, least / len(split), high / len(split))
        level = level * jnp.repeat(jnp.exp(steps), extent[axis_at] // shards_of).reshape((-1,) + (1,) * (len(extent) - 1 - axis_at))
    return level


def normal_values(stream_key, dims, deviation, limit, pieces=(), kind=jnp.bfloat16):
    drawn = jax.random.normal(stream_key, dims, jnp.float32) * deviation
    if len(pieces) > 0:
        drawn = levels(stream_key, dims, pieces, -0.22, 0.18) * drawn
    return jnp.clip(drawn, min=-limit, max=limit).astype(kind)


def setup_inputs(seed: int = 0) -> dict:
    arg_keys = jax.random.split(jax.random.key(seed), 7)
    return {
        "latents": normal_values(arg_keys[0], (MEMBERS, BATCH, CROP, CROP, CH_IN), 1.0, 6.0, ((0, 8), (1, 16))),
        "cotangent": normal_values(arg_keys[1], (MEMBERS, BATCH, CROP, CROP, CH_OUT), 1.0, 6.0, ((0, 8), (1, 16))),
        "weights": normal_values(arg_keys[2], (MEMBERS, CH_IN, 9 * CH_OUT), 1.0, 6.0, ((0, 8), (1, 16)), jnp.float32),
        "first_moment": normal_values(arg_keys[3], (MEMBERS, CH_IN, 9 * CH_OUT), 0.2, 1.2, ((0, 8), (1, 16)), jnp.float32),
        "second_moment": jnp.clip(jnp.exp(math.log(0.5) - 3.218876 * jax.random.uniform(arg_keys[4], (MEMBERS, CH_IN, 9 * CH_OUT), jnp.float32) ** levels(arg_keys[4], (MEMBERS, CH_IN, 9 * CH_OUT), ((0, 8), (1, 16)), -0.2, 0.2)), 0.02, 0.5),
        "sources": draw_sources(jax.random.fold_in(arg_keys[6], 71), 0),
    }


BETA_ONE = 0.9
BETA_TWO = 0.99
RATE = 0.05
EPSILON = 1e-08

def silu_slope(values):
    sig = jax.nn.sigmoid(values)
    return sig * (1.0 + values * (1.0 - sig))

def forward_taps(activation, kernel_bf):
    side_cells = activation.shape[1]
    cell_count = activation.shape[0] * side_cells * side_cells
    cols_out = kernel_bf.shape[1] // 9
    padded = jnp.pad(activation, ((0, 0), (1, 1), (1, 1), (0, 0)))
    summed = jnp.zeros((cell_count, cols_out), jnp.float32)
    for tap_index in range(9):
        tap_row = tap_index // 3
        tap_col = tap_index % 3
        window = padded[:, tap_row:tap_row + side_cells, tap_col:tap_col + side_cells, :].reshape(cell_count, activation.shape[3])
        summed = summed + jnp.dot(window, kernel_bf[:, tap_index * cols_out:(tap_index + 1) * cols_out], preferred_element_type=jnp.float32)
    return summed

def backward_taps(deltas, kernel_bf):
    side_cells = deltas.shape[1]
    cell_count = deltas.shape[0] * side_cells * side_cells
    cols_out = deltas.shape[3]
    padded = jnp.pad(deltas, ((0, 0), (1, 1), (1, 1), (0, 0)))
    summed = jnp.zeros((cell_count, kernel_bf.shape[0]), jnp.float32)
    for tap_index in range(9):
        tap_row = tap_index // 3
        tap_col = tap_index % 3
        window = padded[:, 2 - tap_row:2 - tap_row + side_cells, 2 - tap_col:2 - tap_col + side_cells, :].reshape(cell_count, cols_out)
        block = kernel_bf[:, tap_index * cols_out:(tap_index + 1) * cols_out]
        summed = summed + lax.dot_general(window, block, (((1,), (1,)), ((), ())), preferred_element_type=jnp.float32)
    return summed

def weight_taps(activation, deltas):
    side_cells = activation.shape[1]
    cell_count = activation.shape[0] * side_cells * side_cells
    flat_deltas = deltas.reshape(cell_count, deltas.shape[3])
    padded = jnp.pad(activation, ((0, 0), (1, 1), (1, 1), (0, 0)))
    blocks = []
    for tap_index in range(9):
        tap_row = tap_index // 3
        tap_col = tap_index % 3
        window = padded[:, tap_row:tap_row + side_cells, tap_col:tap_col + side_cells, :].reshape(cell_count, activation.shape[3])
        blocks.append(lax.dot_general(window, flat_deltas, (((0,), (0,)), ((), ())), preferred_element_type=jnp.float32))
    return jnp.concatenate(blocks, axis=1)

def adam_update(weights_now, first_now, second_now, gradient):
    first_new = BETA_ONE * first_now + (1.0 - BETA_ONE) * gradient
    second_new = BETA_TWO * second_now + (1.0 - BETA_TWO) * gradient * gradient
    first_fix = 1.0 - BETA_ONE ** ADAM_STEP
    second_fix = 1.0 - BETA_TWO ** ADAM_STEP
    updated = weights_now - RATE * (first_new / first_fix) / (jnp.sqrt(second_new / second_fix) + EPSILON)
    return (updated, first_new, second_new)

def member_step(inputs):
    latents_one, cotangent_one, weights_one, first_one, second_one = inputs
    scale = (9 * CH_IN) ** (-0.5)
    activation = jax.nn.silu(latents_one.astype(jnp.float32)).astype(jnp.bfloat16)
    kernel_bf = weights_one.astype(jnp.bfloat16)
    hidden = scale * forward_taps(activation, kernel_bf)
    cell_count = hidden.shape[0]
    deltas = (cotangent_one.reshape(cell_count, CH_OUT).astype(jnp.float32) * silu_slope(hidden)).astype(jnp.bfloat16)
    deltas_img = deltas.reshape(cotangent_one.shape)
    back = scale * backward_taps(deltas_img, kernel_bf)
    slope_in = silu_slope(latents_one.reshape(cell_count, CH_IN).astype(jnp.float32))
    latent_grad = (back * slope_in).astype(jnp.bfloat16).reshape(latents_one.shape)
    act_blocks = activation.reshape((N_DP, IMG_DEV) + activation.shape[1:])
    delta_blocks = deltas_img.reshape((N_DP, IMG_DEV) + deltas_img.shape[1:])

    def accumulate(carry, pair):
        part = (scale * weight_taps(pair[0], pair[1])).astype(jnp.bfloat16)
        part = lax.optimization_barrier(part)
        return (carry + part.astype(jnp.float32), None)
    start_sum = jnp.zeros((CH_IN, 9 * CH_OUT), jnp.float32)
    gradient, _ = lax.scan(accumulate, start_sum, (act_blocks, delta_blocks))
    updated, first_new, second_new = adam_update(weights_one, first_one, second_one, gradient)
    return (latent_grad, updated, first_new, second_new)

def reference(latents, cotangent, weights, first_moment, second_moment, sources):
    latent_grad, updated, first_new, second_new = lax.map(member_step, (latents, cotangent, weights, first_moment, second_moment))
    picks = sources.astype(jnp.int32)
    new_weights = jnp.take(updated, picks, axis=0)
    new_first = jnp.take(first_new, picks, axis=0)
    new_second = jnp.take(second_new, picks, axis=0)
    return (latent_grad, new_weights, new_first, new_second)
```

```python
import jax
import jax.numpy as jnp
from jax import lax
from jax.sharding import Mesh
from jax.sharding import PartitionSpec as P

CH_IN = 640
ADAM_STEP = 10


BETA_ONE = 0.9
BETA_TWO = 0.99
RATE = 0.05
EPSILON = 1e-08

MEMBER_AXES = ("x_hi", "z")
DP_AXES = ("x_lo", "y", "core")
TAP_GROUPS = ((0, 1, 2), (3, 4, 5), (6, 7, 8))


def silu_slope(values):
    sig = jax.nn.sigmoid(values)
    return sig * (1.0 + values * (1.0 - sig))


def shifted(padded, tap_index, side_cells, flip):
    tap_row = tap_index // 3
    tap_col = tap_index % 3
    if flip:
        tap_row = 2 - tap_row
        tap_col = 2 - tap_col
    window = padded[:, tap_row : tap_row + side_cells, tap_col : tap_col + side_cells, :]
    return window.reshape(-1, padded.shape[3])


def adam_update(weights_now, first_now, second_now, gradient):
    first_new = BETA_ONE * first_now + (1.0 - BETA_ONE) * gradient
    second_new = BETA_TWO * second_now + (1.0 - BETA_TWO) * gradient * gradient
    first_fix = 1.0 - BETA_ONE**ADAM_STEP
    second_fix = 1.0 - BETA_TWO**ADAM_STEP
    updated = weights_now - RATE * (first_new / first_fix) / (
        jnp.sqrt(second_new / second_fix) + EPSILON
    )
    return (updated, first_new, second_new)


def relocate(stacked, sources):
    members = lax.axis_size(MEMBER_AXES)
    layers = stacked.shape[0]
    shaped = stacked.reshape(layers, members, stacked.shape[1] // members, stacked.shape[2])
    held = lax.all_to_all(shaped, MEMBER_AXES, split_axis=1, concat_axis=1, tiled=True)
    picked = jnp.take(held, sources, axis=1)
    returned = lax.all_to_all(picked, MEMBER_AXES, split_axis=1, concat_axis=1, tiled=True)
    return returned.reshape(stacked.shape)


def gather_rows(rows):
    out = lax.all_gather(rows, "x_lo", axis=0, tiled=False)
    out = lax.all_gather(out, "y", axis=1, tiled=False)
    out = lax.all_gather(out, "core", axis=2, tiled=False)
    return out.reshape(-1, rows.shape[-1])


def scatter_rows(full):
    shaped = lax.psum_scatter(full, "core", scatter_dimension=0, tiled=True)
    shaped = lax.psum_scatter(shaped, "y", scatter_dimension=0, tiled=True)
    return lax.psum_scatter(shaped, "x_lo", scatter_dimension=0, tiled=True)


def local(latents, cotangent, weights, first_moment, second_moment, sources):
    scale = (9 * CH_IN) ** (-0.5)
    n_xlo = lax.axis_size("x_lo")
    n_y = lax.axis_size("y")
    n_core = lax.axis_size("core")
    images = latents[0]
    side_cells = images.shape[1]
    cell_count = images.shape[0] * side_cells * side_cells
    cols_out = cotangent.shape[4]

    moved_state = relocate(jnp.stack([weights[0], first_moment[0], second_moment[0]]), sources)

    activation = jax.nn.silu(images.astype(jnp.float32)).astype(jnp.bfloat16)
    kernel_rows = weights[0].astype(jnp.bfloat16)
    kernel_groups = []
    for group in TAP_GROUPS:
        lo = group[0] * cols_out
        hi = (group[-1] + 1) * cols_out
        kernel_groups.append(gather_rows(kernel_rows[:, lo:hi]))

    padded_act = jnp.pad(activation, ((0, 0), (1, 1), (1, 1), (0, 0)))
    summed = jnp.zeros((cell_count, cols_out), jnp.float32)
    for g, group in enumerate(TAP_GROUPS):
        for t, tap_index in enumerate(group):
            summed = summed + jnp.dot(
                shifted(padded_act, tap_index, side_cells, False),
                kernel_groups[g][:, t * cols_out : (t + 1) * cols_out],
                preferred_element_type=jnp.float32,
            )
    hidden = scale * summed
    deltas = (
        cotangent[0].reshape(cell_count, cols_out).astype(jnp.float32) * silu_slope(hidden)
    ).astype(jnp.bfloat16)
    deltas_img = deltas.reshape(cotangent[0].shape)

    lead = padded_act.shape[:3]
    padded_perm = (
        padded_act.reshape(lead + (n_xlo, n_y, n_core, -1))
        .transpose(0, 1, 2, 5, 4, 3, 6)
        .reshape(padded_act.shape)
    )
    grad_groups = []
    for g, group in enumerate(TAP_GROUPS):
        blocks = []
        for tap_index in group:
            blocks.append(
                lax.dot_general(
                    shifted(padded_perm, tap_index, side_cells, False),
                    deltas,
                    (((0,), (0,)), ((), ())),
                    preferred_element_type=jnp.float32,
                )
            )
        part = (scale * jnp.concatenate(blocks, axis=1)).astype(jnp.bfloat16)
        grad_groups.append(scatter_rows(part))

    padded_del = jnp.pad(deltas_img, ((0, 0), (1, 1), (1, 1), (0, 0)))
    back = jnp.zeros((cell_count, images.shape[3]), jnp.float32)
    for g, group in enumerate(TAP_GROUPS):
        for t, tap_index in enumerate(group):
            back = back + lax.dot_general(
                shifted(padded_del, tap_index, side_cells, True),
                kernel_groups[g][:, t * cols_out : (t + 1) * cols_out],
                (((1,), (1,)), ((), ())),
                preferred_element_type=jnp.float32,
            )
    back = scale * back
    slope_in = silu_slope(images.reshape(cell_count, images.shape[3]).astype(jnp.float32))
    latent_grad = (back * slope_in).astype(jnp.bfloat16).reshape(latents.shape)

    gradient_bf = jnp.concatenate(grad_groups, axis=1)
    moved_grad = relocate(gradient_bf[None], sources)[0].astype(jnp.float32)
    updated, first_new, second_new = adam_update(
        moved_state[0], moved_state[1], moved_state[2], moved_grad
    )
    return (latent_grad, updated[None], first_new[None], second_new[None])


def solution(mesh):
    sub_mesh = Mesh(
        mesh.devices.reshape(2, mesh.shape["member"] // 2, 2, mesh.shape["dp"] // 4, 2),
        MEMBER_AXES + DP_AXES,
    )
    big = P(MEMBER_AXES, DP_AXES, None, None, None)
    state = P(MEMBER_AXES, DP_AXES, None)
    in_specs = (big, big, state, state, state, P())
    out_specs = (big, state, state, state)
    return jax.shard_map(local, mesh=sub_mesh, in_specs=in_specs, out_specs=out_specs, check_vma=False)
```

```python
import jax
import jax.numpy as jnp
from jax import lax
from jax.sharding import Mesh
from jax.sharding import PartitionSpec as P

CH_IN = 640
ADAM_STEP = 10


BETA_ONE = 0.9
BETA_TWO = 0.99
RATE = 0.05
EPSILON = 1e-08

MEMBER_AXES = ("x_hi", "z")
DP_AXES = ("x_lo", "y", "core")
TAP_GROUPS = ((0, 1, 2), (3, 4, 5), (6, 7, 8))


def silu_slope(values):
    sig = jax.nn.sigmoid(values)
    return sig * (1.0 + values * (1.0 - sig))


def shifted(padded, tap_index, side_cells, flip):
    tap_row = tap_index // 3
    tap_col = tap_index % 3
    if flip:
        tap_row = 2 - tap_row
        tap_col = 2 - tap_col
    window = padded[:, tap_row : tap_row + side_cells, tap_col : tap_col + side_cells, :]
    return window.reshape(-1, padded.shape[3])


def adam_update(weights_now, first_now, second_now, gradient):
    first_new = BETA_ONE * first_now + (1.0 - BETA_ONE) * gradient
    second_new = BETA_TWO * second_now + (1.0 - BETA_TWO) * gradient * gradient
    first_fix = 1.0 - BETA_ONE**ADAM_STEP
    second_fix = 1.0 - BETA_TWO**ADAM_STEP
    updated = weights_now - RATE * (first_new / first_fix) / (
        jnp.sqrt(second_new / second_fix) + EPSILON
    )
    return (updated, first_new, second_new)


def to_holders(stacked):
    members = lax.axis_size(MEMBER_AXES)
    layers = stacked.shape[0]
    shaped = stacked.reshape(layers, members, stacked.shape[1] // members, stacked.shape[2])
    return lax.all_to_all(shaped, MEMBER_AXES, split_axis=1, concat_axis=1, tiled=True)


def from_holders(held, sources):
    picked = jnp.take(held, sources, axis=1)
    returned = lax.all_to_all(picked, MEMBER_AXES, split_axis=1, concat_axis=1, tiled=True)
    return returned.reshape(returned.shape[0], -1, returned.shape[3])


def relocate(stacked, sources):
    return from_holders(to_holders(stacked), sources)


def gather_rows(rows):
    return lax.all_gather(rows, DP_AXES, axis=0, tiled=True)


def scatter_rows(full):
    n_dp = lax.axis_size(DP_AXES)
    blocks = full.reshape(n_dp, full.shape[0] // n_dp, full.shape[1])
    return lax.psum_scatter(blocks, DP_AXES, scatter_dimension=0, tiled=True)[0]


def local(latents, cotangent, weights, first_moment, second_moment, sources):
    scale = (9 * CH_IN) ** (-0.5)
    images = latents[0]
    side_cells = images.shape[1]
    cell_count = images.shape[0] * side_cells * side_cells
    cols_out = cotangent.shape[4]

    held_state = to_holders(jnp.stack([weights[0], first_moment[0], second_moment[0]]))

    activation = jax.nn.silu(images.astype(jnp.float32)).astype(jnp.bfloat16)
    kernel_rows = weights[0].astype(jnp.bfloat16)
    kernel_groups = []
    for group in TAP_GROUPS:
        lo = group[0] * cols_out
        hi = (group[-1] + 1) * cols_out
        kernel_groups.append(gather_rows(kernel_rows[:, lo:hi]))

    padded_act = jnp.pad(activation, ((0, 0), (1, 1), (1, 1), (0, 0)))
    held_state, padded_act = lax.optimization_barrier((held_state, padded_act))
    moved_state = from_holders(held_state, sources)
    summed = jnp.zeros((cell_count, cols_out), jnp.float32)
    for g, group in enumerate(TAP_GROUPS):
        for t, tap_index in enumerate(group):
            summed = summed + jnp.dot(
                shifted(padded_act, tap_index, side_cells, False),
                kernel_groups[g][:, t * cols_out : (t + 1) * cols_out],
                preferred_element_type=jnp.float32,
            )
    hidden = scale * summed
    deltas = (
        cotangent[0].reshape(cell_count, cols_out).astype(jnp.float32) * silu_slope(hidden)
    ).astype(jnp.bfloat16)
    moved_state, deltas = lax.optimization_barrier((moved_state, deltas))
    deltas_img = deltas.reshape(cotangent[0].shape)

    grad_groups = []
    for g, group in enumerate(TAP_GROUPS):
        blocks = []
        for tap_index in group:
            blocks.append(
                lax.dot_general(
                    shifted(padded_act, tap_index, side_cells, False),
                    deltas,
                    (((0,), (0,)), ((), ())),
                    preferred_element_type=jnp.float32,
                )
            )
        part = (scale * jnp.concatenate(blocks, axis=1)).astype(jnp.bfloat16)
        grad_groups.append(scatter_rows(part))

    padded_del = jnp.pad(deltas_img, ((0, 0), (1, 1), (1, 1), (0, 0)))
    back = jnp.zeros((cell_count, images.shape[3]), jnp.float32)
    for g, group in enumerate(TAP_GROUPS):
        for t, tap_index in enumerate(group):
            back = back + lax.dot_general(
                shifted(padded_del, tap_index, side_cells, True),
                kernel_groups[g][:, t * cols_out : (t + 1) * cols_out],
                (((1,), (1,)), ((), ())),
                preferred_element_type=jnp.float32,
            )
    back = scale * back
    slope_in = silu_slope(images.reshape(cell_count, images.shape[3]).astype(jnp.float32))
    latent_grad = (back * slope_in).astype(jnp.bfloat16).reshape(latents.shape)

    gradient_bf = jnp.concatenate(grad_groups, axis=1)
    moved_grad = relocate(gradient_bf[None], sources)[0].astype(jnp.float32)
    updated, first_new, second_new = adam_update(
        moved_state[0], moved_state[1], moved_state[2], moved_grad
    )
    return (latent_grad, updated[None], first_new[None], second_new[None])


def solution(mesh):
    sub_mesh = Mesh(
        mesh.devices.reshape(2, mesh.shape["member"] // 2, 2, mesh.shape["dp"] // 4, 2),
        MEMBER_AXES + DP_AXES,
    )
    big = P(MEMBER_AXES, DP_AXES, None, None, None)
    state = P(MEMBER_AXES, DP_AXES, None)
    in_specs = (big, big, state, state, state, P())
    out_specs = (big, state, state, state)
    return jax.shard_map(local, mesh=sub_mesh, in_specs=in_specs, out_specs=out_specs, check_vma=False)
```

```python
import jax
import jax.numpy as jnp
from jax import lax
from jax.sharding import Mesh
from jax.sharding import PartitionSpec as P

CH_IN = 640
ADAM_STEP = 10


BETA_ONE = 0.9
BETA_TWO = 0.99
RATE = 0.05
EPSILON = 1e-08

MEMBER_AXES = ("x_hi", "z")
DP_AXES = ("x_lo", "y", "core")
TAP_GROUPS = ((0, 1, 2), (3, 4, 5), (6, 7, 8))


def silu_slope(values):
    sig = jax.nn.sigmoid(values)
    return sig * (1.0 + values * (1.0 - sig))


def shifted(padded, tap_index, side_cells, flip):
    tap_row = tap_index // 3
    tap_col = tap_index % 3
    if flip:
        tap_row = 2 - tap_row
        tap_col = 2 - tap_col
    window = padded[:, tap_row : tap_row + side_cells, tap_col : tap_col + side_cells, :]
    return window.reshape(-1, padded.shape[3])


def adam_update(weights_now, first_now, second_now, gradient):
    first_new = BETA_ONE * first_now + (1.0 - BETA_ONE) * gradient
    second_new = BETA_TWO * second_now + (1.0 - BETA_TWO) * gradient * gradient
    first_fix = 1.0 - BETA_ONE**ADAM_STEP
    second_fix = 1.0 - BETA_TWO**ADAM_STEP
    updated = weights_now - RATE * (first_new / first_fix) / (
        jnp.sqrt(second_new / second_fix) + EPSILON
    )
    return (updated, first_new, second_new)


def to_holders(stacked):
    members = lax.axis_size(MEMBER_AXES)
    layers = stacked.shape[0]
    shaped = stacked.reshape(layers, members, stacked.shape[1] // members, stacked.shape[2])
    return lax.all_to_all(shaped, MEMBER_AXES, split_axis=1, concat_axis=1, tiled=True)


def from_holders(held, sources):
    picked = jnp.take(held, sources, axis=1)
    returned = lax.all_to_all(picked, MEMBER_AXES, split_axis=1, concat_axis=1, tiled=True)
    return returned.reshape(returned.shape[0], -1, returned.shape[3])


def swap(value, axis):
    return lax.ppermute(value, axis, [(0, 1), (1, 0)])


def weight_rows(padded_sel, deltas, group, side_cells, scale):
    blocks = []
    for tap_index in group:
        blocks.append(
            lax.dot_general(
                shifted(padded_sel, tap_index, side_cells, False),
                deltas,
                (((0,), (0,)), ((), ())),
                preferred_element_type=jnp.float32,
            )
        )
    return (scale * jnp.concatenate(blocks, axis=1)).astype(jnp.bfloat16)


def reduce_group(act_other, act_mine, deltas, group, side_cells, scale, n_xlo, n_y):
    my_y = lax.axis_index("y")
    my_x = lax.axis_index("x_lo")
    sent = swap(weight_rows(act_other, deltas, group, side_cells, scale), "core")
    mine = weight_rows(act_mine, deltas, group, side_cells, scale)
    stage1 = (mine.astype(jnp.float32) + sent.astype(jnp.float32)).astype(jnp.bfloat16)
    stage1 = stage1.reshape(n_xlo, n_y, -1, stage1.shape[1])
    total = lax.dynamic_index_in_dim(stage1, my_y, axis=1, keepdims=False).astype(jnp.float32)
    for step in range(1, n_y):
        piece = lax.dynamic_index_in_dim(stage1, (my_y + step) % n_y, axis=1, keepdims=False)
        got = lax.ppermute(piece, "y", [(i, (i + step) % n_y) for i in range(n_y)])
        total = total + got.astype(jnp.float32)
    stage2 = total.astype(jnp.bfloat16)
    keep = lax.dynamic_index_in_dim(stage2, my_x, axis=0, keepdims=False)
    give = lax.dynamic_index_in_dim(stage2, 1 - my_x, axis=0, keepdims=False)
    return keep.astype(jnp.float32) + swap(give, "x_lo").astype(jnp.float32)


def local(latents, cotangent, weights, first_moment, second_moment, sources):
    scale = (9 * CH_IN) ** (-0.5)
    n_xlo = lax.axis_size("x_lo")
    n_y = lax.axis_size("y")
    n_core = lax.axis_size("core")
    images = latents[0]
    side_cells = images.shape[1]
    cell_count = images.shape[0] * side_cells * side_cells
    cols_out = cotangent.shape[4]

    held_state = to_holders(jnp.stack([weights[0], first_moment[0], second_moment[0]]))

    activation = jax.nn.silu(images.astype(jnp.float32)).astype(jnp.bfloat16)
    kernel_all = lax.all_gather(weights[0].astype(jnp.bfloat16), DP_AXES, axis=0, tiled=True)

    padded_act = jnp.pad(activation, ((0, 0), (1, 1), (1, 1), (0, 0)))
    held_state, padded_act = lax.optimization_barrier((held_state, padded_act))
    moved_state = from_holders(held_state, sources)
    summed = jnp.zeros((cell_count, cols_out), jnp.float32)
    for tap_index in range(9):
        summed = summed + jnp.dot(
            shifted(padded_act, tap_index, side_cells, False),
            kernel_all[:, tap_index * cols_out : (tap_index + 1) * cols_out],
            preferred_element_type=jnp.float32,
        )
    hidden = scale * summed
    deltas = (
        cotangent[0].reshape(cell_count, cols_out).astype(jnp.float32) * silu_slope(hidden)
    ).astype(jnp.bfloat16)
    moved_state, deltas = lax.optimization_barrier((moved_state, deltas))
    deltas_img = deltas.reshape(cotangent[0].shape)

    my_core = lax.axis_index("core")
    lead = padded_act.shape[:3]
    by_core = padded_act.reshape(lead + (n_xlo, n_y, n_core, -1))
    act_mine = lax.dynamic_index_in_dim(by_core, my_core, axis=5, keepdims=False)
    act_other = lax.dynamic_index_in_dim(by_core, 1 - my_core, axis=5, keepdims=False)
    act_mine = act_mine.reshape(lead + (-1,))
    act_other = act_other.reshape(lead + (-1,))
    grad_groups = []
    for group in TAP_GROUPS:
        grad_groups.append(
            reduce_group(act_other, act_mine, deltas, group, side_cells, scale, n_xlo, n_y)
        )

    padded_del = jnp.pad(deltas_img, ((0, 0), (1, 1), (1, 1), (0, 0)))
    back = jnp.zeros((cell_count, images.shape[3]), jnp.float32)
    for tap_index in range(9):
        back = back + lax.dot_general(
            shifted(padded_del, tap_index, side_cells, True),
            kernel_all[:, tap_index * cols_out : (tap_index + 1) * cols_out],
            (((1,), (1,)), ((), ())),
            preferred_element_type=jnp.float32,
        )
    back = scale * back
    slope_in = silu_slope(images.reshape(cell_count, images.shape[3]).astype(jnp.float32))
    latent_grad = (back * slope_in).astype(jnp.bfloat16).reshape(latents.shape)

    gradient = jnp.concatenate(grad_groups, axis=1)
    moved_grad = from_holders(to_holders(gradient[None]), sources)[0]
    updated, first_new, second_new = adam_update(
        moved_state[0], moved_state[1], moved_state[2], moved_grad
    )
    return (latent_grad, updated[None], first_new[None], second_new[None])


def solution(mesh):
    sub_mesh = Mesh(
        mesh.devices.reshape(2, mesh.shape["member"] // 2, 2, mesh.shape["dp"] // 4, 2),
        MEMBER_AXES + DP_AXES,
    )
    big = P(MEMBER_AXES, DP_AXES, None, None, None)
    state = P(MEMBER_AXES, DP_AXES, None)
    in_specs = (big, big, state, state, state, P())
    out_specs = (big, state, state, state)
    return jax.shard_map(local, mesh=sub_mesh, in_specs=in_specs, out_specs=out_specs, check_vma=False)
```

```python
import jax
import jax.numpy as jnp
from jax import lax
from jax.sharding import Mesh
from jax.sharding import PartitionSpec as P

CH_IN = 640
ADAM_STEP = 10


BETA_ONE = 0.9
BETA_TWO = 0.99
RATE = 0.05
EPSILON = 1e-08

MEMBER_AXES = ("x_hi", "z")
DP_AXES = ("x_lo", "y", "core")
TAP_GROUPS = ((0, 1, 2), (3, 4, 5), (6, 7, 8))


def silu_slope(values):
    sig = jax.nn.sigmoid(values)
    return sig * (1.0 + values * (1.0 - sig))


def shifted(padded, tap_index, side_cells, flip):
    tap_row = tap_index // 3
    tap_col = tap_index % 3
    if flip:
        tap_row = 2 - tap_row
        tap_col = 2 - tap_col
    window = padded[:, tap_row : tap_row + side_cells, tap_col : tap_col + side_cells, :]
    return window.reshape(-1, padded.shape[3])


def adam_update(weights_now, first_now, second_now, gradient):
    first_new = BETA_ONE * first_now + (1.0 - BETA_ONE) * gradient
    second_new = BETA_TWO * second_now + (1.0 - BETA_TWO) * gradient * gradient
    first_fix = 1.0 - BETA_ONE**ADAM_STEP
    second_fix = 1.0 - BETA_TWO**ADAM_STEP
    updated = weights_now - RATE * (first_new / first_fix) / (
        jnp.sqrt(second_new / second_fix) + EPSILON
    )
    return (updated, first_new, second_new)


def to_holders(stacked):
    members = lax.axis_size(MEMBER_AXES)
    layers = stacked.shape[0]
    shaped = stacked.reshape(layers, members, stacked.shape[1] // members, stacked.shape[2])
    return lax.all_to_all(shaped, MEMBER_AXES, split_axis=1, concat_axis=1, tiled=True)


def from_holders(held, sources):
    picked = jnp.stack(
        [lax.dynamic_index_in_dim(held, sources[k], axis=1, keepdims=False) for k in range(held.shape[1])],
        axis=1,
    )
    returned = lax.all_to_all(picked, MEMBER_AXES, split_axis=1, concat_axis=1, tiled=True)
    return returned.reshape(returned.shape[0], -1, returned.shape[3])


def swap(value, axis):
    return lax.ppermute(value, axis, [(0, 1), (1, 0)])


def weight_rows(padded_sel, deltas, group, side_cells, scale):
    blocks = []
    for tap_index in group:
        blocks.append(
            lax.dot_general(
                shifted(padded_sel, tap_index, side_cells, False),
                deltas,
                (((0,), (0,)), ((), ())),
                preferred_element_type=jnp.float32,
            )
        )
    return (scale * jnp.concatenate(blocks, axis=1)).astype(jnp.bfloat16)


def core_stage(part, n_xlo, n_y, n_core):
    my_core = lax.axis_index("core")
    part = part.reshape(n_xlo, n_y, n_core, -1, part.shape[1])
    keep = lax.dynamic_index_in_dim(part, my_core, axis=2, keepdims=False)
    give = lax.dynamic_index_in_dim(part, 1 - my_core, axis=2, keepdims=False)
    return (keep.astype(jnp.float32) + swap(give, "core").astype(jnp.float32)).astype(
        jnp.bfloat16
    )


def ring_stages(stage1, n_y):
    my_y = lax.axis_index("y")
    my_x = lax.axis_index("x_lo")
    total = lax.dynamic_index_in_dim(stage1, my_y, axis=1, keepdims=False).astype(jnp.float32)
    for step in range(1, n_y):
        piece = lax.dynamic_index_in_dim(stage1, (my_y + step) % n_y, axis=1, keepdims=False)
        got = lax.ppermute(piece, "y", [(i, (i + step) % n_y) for i in range(n_y)])
        total = total + got.astype(jnp.float32)
    stage2 = total.astype(jnp.bfloat16)
    keep = lax.dynamic_index_in_dim(stage2, my_x, axis=0, keepdims=False)
    give = lax.dynamic_index_in_dim(stage2, 1 - my_x, axis=0, keepdims=False)
    return keep.astype(jnp.float32) + swap(give, "x_lo").astype(jnp.float32)


def local(latents, cotangent, weights, first_moment, second_moment, sources):
    scale = (9 * CH_IN) ** (-0.5)
    n_xlo = lax.axis_size("x_lo")
    n_y = lax.axis_size("y")
    n_core = lax.axis_size("core")
    images = latents[0]
    side_cells = images.shape[1]
    cell_count = images.shape[0] * side_cells * side_cells
    cols_out = cotangent.shape[4]

    held_state = to_holders(jnp.stack([weights[0], first_moment[0], second_moment[0]]))

    activation = jax.nn.silu(images.astype(jnp.float32)).astype(jnp.bfloat16)
    kernel_all = lax.all_gather(weights[0].astype(jnp.bfloat16), DP_AXES, axis=0, tiled=True)

    padded_act = jnp.pad(activation, ((0, 0), (1, 1), (1, 1), (0, 0)))
    held_state, padded_act = lax.optimization_barrier((held_state, padded_act))
    moved_state = from_holders(held_state, sources)
    summed = jnp.zeros((cell_count, cols_out), jnp.float32)
    for tap_index in range(9):
        summed = summed + jnp.dot(
            shifted(padded_act, tap_index, side_cells, False),
            kernel_all[:, tap_index * cols_out : (tap_index + 1) * cols_out],
            preferred_element_type=jnp.float32,
        )
    hidden = scale * summed
    deltas = (
        cotangent[0].reshape(cell_count, cols_out).astype(jnp.float32) * silu_slope(hidden)
    ).astype(jnp.bfloat16)
    moved_state, deltas = lax.optimization_barrier((moved_state, deltas))
    deltas_img = deltas.reshape(cotangent[0].shape)

    firsts = []
    for group in TAP_GROUPS:
        part = weight_rows(padded_act, deltas, group, side_cells, scale)
        firsts.append(core_stage(part, n_xlo, n_y, n_core))

    padded_del = jnp.pad(deltas_img, ((0, 0), (1, 1), (1, 1), (0, 0)))
    padded_del, firsts = lax.optimization_barrier((padded_del, firsts))
    grad_groups = [ring_stages(first, n_y) for first in firsts]
    back = jnp.zeros((cell_count, images.shape[3]), jnp.float32)
    for tap_index in range(9):
        back = back + lax.dot_general(
            shifted(padded_del, tap_index, side_cells, True),
            kernel_all[:, tap_index * cols_out : (tap_index + 1) * cols_out],
            (((1,), (1,)), ((), ())),
            preferred_element_type=jnp.float32,
        )
    back = scale * back
    slope_in = silu_slope(images.reshape(cell_count, images.shape[3]).astype(jnp.float32))
    latent_grad = (back * slope_in).astype(jnp.bfloat16).reshape(latents.shape)

    gradient = jnp.concatenate(grad_groups, axis=1)
    moved_grad = from_holders(to_holders(gradient[None]), sources)[0]
    updated, first_new, second_new = adam_update(
        moved_state[0], moved_state[1], moved_state[2], moved_grad
    )
    return (latent_grad, updated[None], first_new[None], second_new[None])


def solution(mesh):
    sub_mesh = Mesh(
        mesh.devices.reshape(2, mesh.shape["member"] // 2, 2, mesh.shape["dp"] // 4, 2),
        MEMBER_AXES + DP_AXES,
    )
    big = P(MEMBER_AXES, DP_AXES, None, None, None)
    state = P(MEMBER_AXES, DP_AXES, None)
    in_specs = (big, big, state, state, state, P())
    out_specs = (big, state, state, state)
    return jax.shard_map(local, mesh=sub_mesh, in_specs=in_specs, out_specs=out_specs, check_vma=False)
```

```python
import jax
import jax.numpy as jnp
from jax import lax
from jax.sharding import Mesh
from jax.sharding import PartitionSpec as P

CH_IN = 640
ADAM_STEP = 10


BETA_ONE = 0.9
BETA_TWO = 0.99
RATE = 0.05
EPSILON = 1e-08

MEMBER_AXES = ("x_hi", "z")
DP_AXES = ("x_lo", "y", "core")
TAP_GROUPS = ((0, 1, 2), (3, 4, 5), (6, 7, 8))


def silu_slope(values):
    sig = jax.nn.sigmoid(values)
    return sig * (1.0 + values * (1.0 - sig))


def shifted(padded, tap_index, side_cells, flip):
    tap_row = tap_index // 3
    tap_col = tap_index % 3
    if flip:
        tap_row = 2 - tap_row
        tap_col = 2 - tap_col
    window = padded[:, tap_row : tap_row + side_cells, tap_col : tap_col + side_cells, :]
    return window.reshape(-1, padded.shape[3])


def adam_update(weights_now, first_now, second_now, gradient):
    first_new = BETA_ONE * first_now + (1.0 - BETA_ONE) * gradient
    second_new = BETA_TWO * second_now + (1.0 - BETA_TWO) * gradient * gradient
    first_fix = 1.0 - BETA_ONE**ADAM_STEP
    second_fix = 1.0 - BETA_TWO**ADAM_STEP
    updated = weights_now - RATE * (first_new / first_fix) / (
        jnp.sqrt(second_new / second_fix) + EPSILON
    )
    return (updated, first_new, second_new)


def to_holders(stacked):
    members = lax.axis_size(MEMBER_AXES)
    layers = stacked.shape[0]
    shaped = stacked.reshape(layers, members, stacked.shape[1] // members, stacked.shape[2])
    return lax.all_to_all(shaped, MEMBER_AXES, split_axis=1, concat_axis=1, tiled=True)


def from_holders(held, sources):
    picked = jnp.stack(
        [lax.dynamic_index_in_dim(held, sources[k], axis=1, keepdims=False) for k in range(held.shape[1])],
        axis=1,
    )
    returned = lax.all_to_all(picked, MEMBER_AXES, split_axis=1, concat_axis=1, tiled=True)
    return returned.reshape(returned.shape[0], -1, returned.shape[3])


def swap(value, axis):
    return lax.ppermute(value, axis, [(0, 1), (1, 0)])


def weight_rows(padded_sel, deltas, group, side_cells, scale):
    blocks = []
    for tap_index in group:
        blocks.append(
            lax.dot_general(
                shifted(padded_sel, tap_index, side_cells, False),
                deltas,
                (((0,), (0,)), ((), ())),
                preferred_element_type=jnp.float32,
            )
        )
    return (scale * jnp.concatenate(blocks, axis=1)).astype(jnp.bfloat16)


def core_stage(part, n_xlo, n_y, n_core):
    my_core = lax.axis_index("core")
    part = part.reshape(n_xlo, n_y, n_core, -1, part.shape[1])
    keep = lax.dynamic_index_in_dim(part, my_core, axis=2, keepdims=False)
    give = lax.dynamic_index_in_dim(part, 1 - my_core, axis=2, keepdims=False)
    return (keep.astype(jnp.float32) + swap(give, "core").astype(jnp.float32)).astype(
        jnp.bfloat16
    )


def ring_stages(stage1, n_y):
    my_y = lax.axis_index("y")
    my_x = lax.axis_index("x_lo")
    total = lax.dynamic_index_in_dim(stage1, my_y, axis=1, keepdims=False).astype(jnp.float32)
    for step in range(1, n_y):
        piece = lax.dynamic_index_in_dim(stage1, (my_y + step) % n_y, axis=1, keepdims=False)
        got = lax.ppermute(piece, "y", [(i, (i + step) % n_y) for i in range(n_y)])
        total = total + got.astype(jnp.float32)
    stage2 = total.astype(jnp.bfloat16)
    keep = lax.dynamic_index_in_dim(stage2, my_x, axis=0, keepdims=False)
    give = lax.dynamic_index_in_dim(stage2, 1 - my_x, axis=0, keepdims=False)
    return keep.astype(jnp.float32) + swap(give, "x_lo").astype(jnp.float32)


def local(latents, cotangent, weights, first_moment, second_moment, sources):
    scale = (9 * CH_IN) ** (-0.5)
    n_xlo = lax.axis_size("x_lo")
    n_y = lax.axis_size("y")
    n_core = lax.axis_size("core")
    images = latents[0]
    side_cells = images.shape[1]
    cell_count = images.shape[0] * side_cells * side_cells
    cols_out = cotangent.shape[4]

    activation = jax.nn.silu(images.astype(jnp.float32)).astype(jnp.bfloat16)
    kernel_all = lax.all_gather(weights[0].astype(jnp.bfloat16), DP_AXES, axis=0, tiled=True)
    padded_act = jnp.pad(activation, ((0, 0), (1, 1), (1, 1), (0, 0)))

    state = jnp.stack([weights[0], first_moment[0], second_moment[0]])
    state, kernel_all = lax.optimization_barrier((state, kernel_all))
    held_state = to_holders(state)
    summed = jnp.zeros((cell_count, cols_out), jnp.float32)
    for tap_index in range(9):
        summed = summed + jnp.dot(
            shifted(padded_act, tap_index, side_cells, False),
            kernel_all[:, tap_index * cols_out : (tap_index + 1) * cols_out],
            preferred_element_type=jnp.float32,
        )
    hidden = scale * summed
    deltas = (
        cotangent[0].reshape(cell_count, cols_out).astype(jnp.float32) * silu_slope(hidden)
    ).astype(jnp.bfloat16)
    held_state, deltas = lax.optimization_barrier((held_state, deltas))
    moved_state = from_holders(held_state, sources)
    deltas_img = deltas.reshape(cotangent[0].shape)

    firsts = []
    for group in TAP_GROUPS:
        part = weight_rows(padded_act, deltas, group, side_cells, scale)
        firsts.append(core_stage(part, n_xlo, n_y, n_core))

    padded_del = jnp.pad(deltas_img, ((0, 0), (1, 1), (1, 1), (0, 0)))
    padded_del, firsts, moved_state = lax.optimization_barrier((padded_del, firsts, moved_state))
    grad_groups = [ring_stages(first, n_y) for first in firsts]
    back = jnp.zeros((cell_count, images.shape[3]), jnp.float32)
    for tap_index in range(9):
        back = back + lax.dot_general(
            shifted(padded_del, tap_index, side_cells, True),
            kernel_all[:, tap_index * cols_out : (tap_index + 1) * cols_out],
            (((1,), (1,)), ((), ())),
            preferred_element_type=jnp.float32,
        )
    back = scale * back
    slope_in = silu_slope(images.reshape(cell_count, images.shape[3]).astype(jnp.float32))
    latent_grad = (back * slope_in).astype(jnp.bfloat16).reshape(latents.shape)

    gradient = jnp.concatenate(grad_groups, axis=1)
    moved_grad = from_holders(to_holders(gradient[None]), sources)[0]
    updated, first_new, second_new = adam_update(
        moved_state[0], moved_state[1], moved_state[2], moved_grad
    )
    return (latent_grad, updated[None], first_new[None], second_new[None])


def solution(mesh):
    sub_mesh = Mesh(
        mesh.devices.reshape(2, mesh.shape["member"] // 2, 2, mesh.shape["dp"] // 4, 2),
        MEMBER_AXES + DP_AXES,
    )
    big = P(MEMBER_AXES, DP_AXES, None, None, None)
    state = P(MEMBER_AXES, DP_AXES, None)
    in_specs = (big, big, state, state, state, P())
    out_specs = (big, state, state, state)
    return jax.shard_map(local, mesh=sub_mesh, in_specs=in_specs, out_specs=out_specs, check_vma=False)
```

```python
import jax
import jax.numpy as jnp
from jax import lax
from jax.sharding import Mesh
from jax.sharding import PartitionSpec as P

CH_IN = 640
ADAM_STEP = 10


BETA_ONE = 0.9
BETA_TWO = 0.99
RATE = 0.05
EPSILON = 1e-08

MEMBER_AXES = ("x_hi", "z")
DP_AXES = ("x_lo", "y", "core")
TAP_GROUPS = ((0, 1, 2), (3, 4, 5), (6, 7, 8))


def silu_slope(values):
    sig = jax.nn.sigmoid(values)
    return sig * (1.0 + values * (1.0 - sig))


def shifted(padded, tap_index, side_cells, flip):
    tap_row = tap_index // 3
    tap_col = tap_index % 3
    if flip:
        tap_row = 2 - tap_row
        tap_col = 2 - tap_col
    window = padded[:, tap_row : tap_row + side_cells, tap_col : tap_col + side_cells, :]
    return window.reshape(-1, padded.shape[3])


def adam_update(weights_now, first_now, second_now, gradient):
    first_new = BETA_ONE * first_now + (1.0 - BETA_ONE) * gradient
    second_new = BETA_TWO * second_now + (1.0 - BETA_TWO) * gradient * gradient
    first_fix = 1.0 - BETA_ONE**ADAM_STEP
    second_fix = 1.0 - BETA_TWO**ADAM_STEP
    updated = weights_now - RATE * (first_new / first_fix) / (
        jnp.sqrt(second_new / second_fix) + EPSILON
    )
    return (updated, first_new, second_new)


def to_holders(stacked):
    members = lax.axis_size(MEMBER_AXES)
    layers, rows, cols = stacked.shape
    shaped = stacked.reshape(layers, members, rows // members, cols).transpose(1, 0, 2, 3)
    shaped = shaped.reshape(members, -1, 128)
    return lax.all_to_all(shaped, MEMBER_AXES, split_axis=0, concat_axis=0, tiled=True)


def from_holders(held, sources, shape):
    members = held.shape[0]
    picked = jnp.stack(
        [lax.dynamic_index_in_dim(held, sources[k], axis=0, keepdims=False) for k in range(members)]
    )
    returned = lax.all_to_all(picked, MEMBER_AXES, split_axis=0, concat_axis=0, tiled=True)
    layers, rows, cols = shape
    returned = returned.reshape(members, layers, rows // members, cols).transpose(1, 0, 2, 3)
    return returned.reshape(shape)


def swap(value, axis):
    return lax.ppermute(value, axis, [(0, 1), (1, 0)])


def weight_rows(padded_sel, deltas, group, side_cells, scale):
    blocks = []
    for tap_index in group:
        blocks.append(
            lax.dot_general(
                shifted(padded_sel, tap_index, side_cells, False),
                deltas,
                (((0,), (0,)), ((), ())),
                preferred_element_type=jnp.float32,
            )
        )
    return (scale * jnp.concatenate(blocks, axis=1)).astype(jnp.bfloat16)


def core_stage(part, n_xlo, n_y, n_core):
    my_core = lax.axis_index("core")
    part = part.reshape(n_xlo, n_y, n_core, -1, part.shape[1])
    keep = lax.dynamic_index_in_dim(part, my_core, axis=2, keepdims=False)
    give = lax.dynamic_index_in_dim(part, 1 - my_core, axis=2, keepdims=False)
    return (keep.astype(jnp.float32) + swap(give, "core").astype(jnp.float32)).astype(
        jnp.bfloat16
    )


def ring_stages(firsts, n_y):
    my_y = lax.axis_index("y")
    my_x = lax.axis_index("x_lo")
    stage1 = jnp.concatenate(firsts, axis=3)
    total = lax.dynamic_index_in_dim(stage1, my_y, axis=1, keepdims=False).astype(jnp.float32)
    for step in range(1, n_y):
        piece = lax.dynamic_index_in_dim(stage1, (my_y + step) % n_y, axis=1, keepdims=False)
        got = lax.ppermute(piece, "y", [(i, (i + step) % n_y) for i in range(n_y)])
        total = total + got.astype(jnp.float32)
    stage2 = total.astype(jnp.bfloat16)
    keep = lax.dynamic_index_in_dim(stage2, my_x, axis=0, keepdims=False)
    give = lax.dynamic_index_in_dim(stage2, 1 - my_x, axis=0, keepdims=False)
    return keep.astype(jnp.float32) + swap(give, "x_lo").astype(jnp.float32)


def local(latents, cotangent, weights, first_moment, second_moment, sources):
    scale = (9 * CH_IN) ** (-0.5)
    n_xlo = lax.axis_size("x_lo")
    n_y = lax.axis_size("y")
    n_core = lax.axis_size("core")
    images = latents[0]
    side_cells = images.shape[1]
    cell_count = images.shape[0] * side_cells * side_cells
    cols_out = cotangent.shape[4]

    activation = jax.nn.silu(images.astype(jnp.float32)).astype(jnp.bfloat16)
    kernel_all = lax.all_gather(weights[0].astype(jnp.bfloat16), DP_AXES, axis=0, tiled=True)
    padded_act = jnp.pad(activation, ((0, 0), (1, 1), (1, 1), (0, 0)))

    state = jnp.stack([weights[0], first_moment[0], second_moment[0]])
    state, kernel_all = lax.optimization_barrier((state, kernel_all))
    held_state = to_holders(state)
    summed = jnp.zeros((cell_count, cols_out), jnp.float32)
    for tap_index in range(9):
        summed = summed + jnp.dot(
            shifted(padded_act, tap_index, side_cells, False),
            kernel_all[:, tap_index * cols_out : (tap_index + 1) * cols_out],
            preferred_element_type=jnp.float32,
        )
    hidden = scale * summed
    deltas = (
        cotangent[0].reshape(cell_count, cols_out).astype(jnp.float32) * silu_slope(hidden)
    ).astype(jnp.bfloat16)
    held_state, deltas = lax.optimization_barrier((held_state, deltas))
    moved_state = from_holders(held_state, sources, state.shape)
    deltas_img = deltas.reshape(cotangent[0].shape)

    firsts = []
    for group in TAP_GROUPS:
        part = weight_rows(padded_act, deltas, group, side_cells, scale)
        firsts.append(core_stage(part, n_xlo, n_y, n_core))

    padded_del = jnp.pad(deltas_img, ((0, 0), (1, 1), (1, 1), (0, 0)))
    padded_del, firsts, moved_state = lax.optimization_barrier((padded_del, firsts, moved_state))
    gradient = ring_stages(firsts, n_y)
    back = jnp.zeros((cell_count, images.shape[3]), jnp.float32)
    for tap_index in range(9):
        back = back + lax.dot_general(
            shifted(padded_del, tap_index, side_cells, True),
            kernel_all[:, tap_index * cols_out : (tap_index + 1) * cols_out],
            (((1,), (1,)), ((), ())),
            preferred_element_type=jnp.float32,
        )
    back = scale * back
    slope_in = silu_slope(images.reshape(cell_count, images.shape[3]).astype(jnp.float32))
    latent_grad = (back * slope_in).astype(jnp.bfloat16).reshape(latents.shape)

    moved_grad = from_holders(to_holders(gradient[None]), sources, (1,) + gradient.shape)[0]
    updated, first_new, second_new = adam_update(
        moved_state[0], moved_state[1], moved_state[2], moved_grad
    )
    return (latent_grad, updated[None], first_new[None], second_new[None])


def solution(mesh):
    sub_mesh = Mesh(
        mesh.devices.reshape(2, mesh.shape["member"] // 2, 2, mesh.shape["dp"] // 4, 2),
        MEMBER_AXES + DP_AXES,
    )
    big = P(MEMBER_AXES, DP_AXES, None, None, None)
    state = P(MEMBER_AXES, DP_AXES, None)
    in_specs = (big, big, state, state, state, P())
    out_specs = (big, state, state, state)
    return jax.shard_map(local, mesh=sub_mesh, in_specs=in_specs, out_specs=out_specs, check_vma=False)
```

```python
import jax
import jax.numpy as jnp
from jax import lax
from jax.sharding import Mesh
from jax.sharding import PartitionSpec as P

CH_IN = 640
ADAM_STEP = 10


BETA_ONE = 0.9
BETA_TWO = 0.99
RATE = 0.05
EPSILON = 1e-08

MEMBER_AXES = ("x_hi", "z")
DP_AXES = ("x_lo", "y", "core")
TAP_GROUPS = ((0, 1, 2), (3, 4, 5), (6, 7, 8))


def silu_slope(values):
    sig = jax.nn.sigmoid(values)
    return sig * (1.0 + values * (1.0 - sig))


def shifted(padded, tap_index, side_cells, flip):
    tap_row = tap_index // 3
    tap_col = tap_index % 3
    if flip:
        tap_row = 2 - tap_row
        tap_col = 2 - tap_col
    window = padded[:, tap_row : tap_row + side_cells, tap_col : tap_col + side_cells, :]
    return window.reshape(-1, padded.shape[3])


def adam_update(weights_now, first_now, second_now, gradient):
    first_new = BETA_ONE * first_now + (1.0 - BETA_ONE) * gradient
    second_new = BETA_TWO * second_now + (1.0 - BETA_TWO) * gradient * gradient
    first_fix = 1.0 - BETA_ONE**ADAM_STEP
    second_fix = 1.0 - BETA_TWO**ADAM_STEP
    updated = weights_now - RATE * (first_new / first_fix) / (
        jnp.sqrt(second_new / second_fix) + EPSILON
    )
    return (updated, first_new, second_new)


def to_holders(stacked):
    members = lax.axis_size(MEMBER_AXES)
    layers = stacked.shape[0]
    shaped = stacked.reshape(layers, members, stacked.shape[1] // members, stacked.shape[2])
    return lax.all_to_all(shaped, MEMBER_AXES, split_axis=1, concat_axis=1, tiled=True)


def from_holders(held, sources):
    picked = jnp.stack(
        [lax.dynamic_index_in_dim(held, sources[k], axis=1, keepdims=False) for k in range(held.shape[1])],
        axis=1,
    )
    returned = lax.all_to_all(picked, MEMBER_AXES, split_axis=1, concat_axis=1, tiled=True)
    return returned.reshape(returned.shape[0], -1, returned.shape[3])


def swap(value, axis):
    return lax.ppermute(value, axis, [(0, 1), (1, 0)])


def weight_rows(padded_sel, deltas, group, side_cells, scale):
    blocks = []
    for tap_index in group:
        blocks.append(
            lax.dot_general(
                shifted(padded_sel, tap_index, side_cells, False),
                deltas,
                (((0,), (0,)), ((), ())),
                preferred_element_type=jnp.float32,
            )
        )
    return (scale * jnp.concatenate(blocks, axis=1)).astype(jnp.bfloat16)


def core_stage(part, n_xlo, n_y, n_core):
    my_core = lax.axis_index("core")
    part = part.reshape(n_xlo, n_y, n_core, -1, part.shape[1])
    keep = lax.dynamic_index_in_dim(part, my_core, axis=2, keepdims=False)
    give = lax.dynamic_index_in_dim(part, 1 - my_core, axis=2, keepdims=False)
    return (keep.astype(jnp.float32) + swap(give, "core").astype(jnp.float32)).astype(
        jnp.bfloat16
    )


def square_halving(stage1, flip_a, flip_b, pairs_a, pairs_b):
    my_y = lax.axis_index("y")
    across_a = flip_a(my_y)
    across_b = flip_b(my_y)
    send_ids = (across_a, flip_a(across_b))
    keep_ids = (my_y, across_b)
    send = jnp.stack([lax.dynamic_index_in_dim(stage1, i, axis=1, keepdims=False) for i in send_ids], 1)
    keep = jnp.stack([lax.dynamic_index_in_dim(stage1, i, axis=1, keepdims=False) for i in keep_ids], 1)
    got = lax.ppermute(send, "y", pairs_a)
    half = (keep.astype(jnp.float32) + got.astype(jnp.float32)).astype(jnp.bfloat16)
    got = lax.ppermute(half[:, 1], "y", pairs_b)
    return half[:, 0].astype(jnp.float32) + got.astype(jnp.float32)


def ring_stages(stage1, n_y):
    my_x = lax.axis_index("x_lo")
    flip_one = lambda y: y + 1 - 2 * (y % 2)
    flip_two = lambda y: n_y - 1 - y
    pairs_one = [(i, flip_one(i)) for i in range(n_y)]
    pairs_two = [(i, flip_two(i)) for i in range(n_y)]
    cols = stage1.shape[-1] // 2
    total = jnp.concatenate(
        [
            square_halving(stage1[..., :cols], flip_one, flip_two, pairs_one, pairs_two),
            square_halving(stage1[..., cols:], flip_two, flip_one, pairs_two, pairs_one),
        ],
        axis=-1,
    )
    stage2 = total.astype(jnp.bfloat16)
    keep = lax.dynamic_index_in_dim(stage2, my_x, axis=0, keepdims=False)
    give = lax.dynamic_index_in_dim(stage2, 1 - my_x, axis=0, keepdims=False)
    return keep.astype(jnp.float32) + swap(give, "x_lo").astype(jnp.float32)


def local(latents, cotangent, weights, first_moment, second_moment, sources):
    scale = (9 * CH_IN) ** (-0.5)
    n_xlo = lax.axis_size("x_lo")
    n_y = lax.axis_size("y")
    n_core = lax.axis_size("core")
    images = latents[0]
    side_cells = images.shape[1]
    cell_count = images.shape[0] * side_cells * side_cells
    cols_out = cotangent.shape[4]

    activation = jax.nn.silu(images.astype(jnp.float32)).astype(jnp.bfloat16)
    kernel_all = lax.all_gather(weights[0].astype(jnp.bfloat16), DP_AXES, axis=0, tiled=True)
    padded_act = jnp.pad(activation, ((0, 0), (1, 1), (1, 1), (0, 0)))

    state = jnp.stack([weights[0], first_moment[0], second_moment[0]])
    state, kernel_all = lax.optimization_barrier((state, kernel_all))
    held_state = to_holders(state)
    summed = jnp.zeros((cell_count, cols_out), jnp.float32)
    for tap_index in range(9):
        summed = summed + jnp.dot(
            shifted(padded_act, tap_index, side_cells, False),
            kernel_all[:, tap_index * cols_out : (tap_index + 1) * cols_out],
            preferred_element_type=jnp.float32,
        )
    hidden = scale * summed
    deltas = (
        cotangent[0].reshape(cell_count, cols_out).astype(jnp.float32) * silu_slope(hidden)
    ).astype(jnp.bfloat16)
    held_state, deltas = lax.optimization_barrier((held_state, deltas))
    moved_state = from_holders(held_state, sources)
    deltas_img = deltas.reshape(cotangent[0].shape)

    firsts = []
    for group in TAP_GROUPS:
        part = weight_rows(padded_act, deltas, group, side_cells, scale)
        firsts.append(core_stage(part, n_xlo, n_y, n_core))

    padded_del = jnp.pad(deltas_img, ((0, 0), (1, 1), (1, 1), (0, 0)))
    padded_del, firsts, moved_state = lax.optimization_barrier((padded_del, firsts, moved_state))
    grad_groups = [ring_stages(first, n_y) for first in firsts]
    back = jnp.zeros((cell_count, images.shape[3]), jnp.float32)
    for tap_index in range(9):
        back = back + lax.dot_general(
            shifted(padded_del, tap_index, side_cells, True),
            kernel_all[:, tap_index * cols_out : (tap_index + 1) * cols_out],
            (((1,), (1,)), ((), ())),
            preferred_element_type=jnp.float32,
        )
    back = scale * back
    slope_in = silu_slope(images.reshape(cell_count, images.shape[3]).astype(jnp.float32))
    latent_grad = (back * slope_in).astype(jnp.bfloat16).reshape(latents.shape)

    gradient = jnp.concatenate(grad_groups, axis=1)
    moved_grad = from_holders(to_holders(gradient[None]), sources)[0]
    updated, first_new, second_new = adam_update(
        moved_state[0], moved_state[1], moved_state[2], moved_grad
    )
    return (latent_grad, updated[None], first_new[None], second_new[None])


def solution(mesh):
    sub_mesh = Mesh(
        mesh.devices.reshape(2, mesh.shape["member"] // 2, 2, mesh.shape["dp"] // 4, 2),
        MEMBER_AXES + DP_AXES,
    )
    big = P(MEMBER_AXES, DP_AXES, None, None, None)
    state = P(MEMBER_AXES, DP_AXES, None)
    in_specs = (big, big, state, state, state, P())
    out_specs = (big, state, state, state)
    return jax.shard_map(local, mesh=sub_mesh, in_specs=in_specs, out_specs=out_specs, check_vma=False)
```

```python
import jax
import jax.numpy as jnp
from jax import lax
from jax.sharding import Mesh
from jax.sharding import PartitionSpec as P


CH_IN = 640
ADAM_STEP = 10


BETA_ONE = 0.9
BETA_TWO = 0.99
RATE = 0.05
EPSILON = 1e-08

MEMBER_AXES = ("x_hi", "z")
DP_AXES = ("x_lo", "y", "core")
TAP_GROUPS = ((0, 1, 2), (3, 4, 5), (6, 7, 8))


def silu_slope(values):
    sig = jax.nn.sigmoid(values)
    return sig * (1.0 + values * (1.0 - sig))


def shifted(padded, tap_index, side_cells, flip):
    tap_row = tap_index // 3
    tap_col = tap_index % 3
    if flip:
        tap_row = 2 - tap_row
        tap_col = 2 - tap_col
    window = padded[:, tap_row : tap_row + side_cells, tap_col : tap_col + side_cells, :]
    return window.reshape(-1, padded.shape[3])


def adam_update(weights_now, first_now, second_now, gradient):
    first_new = BETA_ONE * first_now + (1.0 - BETA_ONE) * gradient
    second_new = BETA_TWO * second_now + (1.0 - BETA_TWO) * gradient * gradient
    first_fix = 1.0 - BETA_ONE**ADAM_STEP
    second_fix = 1.0 - BETA_TWO**ADAM_STEP
    updated = weights_now - RATE * (first_new / first_fix) / (
        jnp.sqrt(second_new / second_fix) + EPSILON
    )
    return (updated, first_new, second_new)


def to_holders(stacked):
    members = lax.axis_size(MEMBER_AXES)
    layers = stacked.shape[0]
    shaped = stacked.reshape(layers, members, stacked.shape[1] // members, stacked.shape[2])
    return lax.all_to_all(shaped, MEMBER_AXES, split_axis=1, concat_axis=1, tiled=True)


def from_holders(held, sources):
    picked = jnp.stack(
        [lax.dynamic_index_in_dim(held, sources[k], axis=1, keepdims=False) for k in range(held.shape[1])],
        axis=1,
    )
    returned = lax.all_to_all(picked, MEMBER_AXES, split_axis=1, concat_axis=1, tiled=True)
    return returned.reshape(returned.shape[0], -1, returned.shape[3])


def swap(value, axis):
    return lax.ppermute(value, axis, [(0, 1), (1, 0)])


def weight_rows(padded_sel, deltas, group, side_cells, scale):
    blocks = []
    for tap_index in group:
        blocks.append(
            lax.dot_general(
                shifted(padded_sel, tap_index, side_cells, False),
                deltas,
                (((0,), (0,)), ((), ())),
                preferred_element_type=jnp.float32,
            )
        )
    return (scale * jnp.concatenate(blocks, axis=1)).astype(jnp.bfloat16)


def core_stage(part, n_xlo, n_y, n_core):
    my_core = lax.axis_index("core")
    part = part.reshape(n_xlo, n_y, n_core, -1, part.shape[1])
    keep = lax.dynamic_index_in_dim(part, my_core, axis=2, keepdims=False)
    give = lax.dynamic_index_in_dim(part, 1 - my_core, axis=2, keepdims=False)
    return (keep.astype(jnp.float32) + swap(give, "core").astype(jnp.float32)).astype(
        jnp.bfloat16
    )


def square_halving(stage1, flip_a, flip_b, pairs_a, pairs_b):
    my_y = lax.axis_index("y")
    across_a = flip_a(my_y)
    across_b = flip_b(my_y)
    send_ids = (across_a, flip_a(across_b))
    keep_ids = (my_y, across_b)
    send = jnp.stack([lax.dynamic_index_in_dim(stage1, i, axis=1, keepdims=False) for i in send_ids], 1)
    keep = jnp.stack([lax.dynamic_index_in_dim(stage1, i, axis=1, keepdims=False) for i in keep_ids], 1)
    got = lax.ppermute(send, "y", pairs_a)
    half = (keep.astype(jnp.float32) + got.astype(jnp.float32)).astype(jnp.bfloat16)
    got = lax.ppermute(half[:, 1], "y", pairs_b)
    return half[:, 0].astype(jnp.float32) + got.astype(jnp.float32)


def ring_stages(stage1, n_y):
    my_x = lax.axis_index("x_lo")
    flip_one = lambda y: y + 1 - 2 * (y % 2)
    flip_two = lambda y: n_y - 1 - y
    pairs_one = [(i, flip_one(i)) for i in range(n_y)]
    pairs_two = [(i, flip_two(i)) for i in range(n_y)]
    cols = stage1.shape[-1] // 2
    total = jnp.concatenate(
        [
            square_halving(stage1[..., :cols], flip_one, flip_two, pairs_one, pairs_two),
            square_halving(stage1[..., cols:], flip_two, flip_one, pairs_two, pairs_one),
        ],
        axis=-1,
    )
    stage2 = total.astype(jnp.bfloat16)
    keep = lax.dynamic_index_in_dim(stage2, my_x, axis=0, keepdims=False)
    give = lax.dynamic_index_in_dim(stage2, 1 - my_x, axis=0, keepdims=False)
    return keep.astype(jnp.float32) + swap(give, "x_lo").astype(jnp.float32)


def step_body(latents, cotangent, weights, first_moment, second_moment, sources):
    scale = (9 * CH_IN) ** (-0.5)
    n_xlo = lax.axis_size("x_lo")
    n_y = lax.axis_size("y")
    n_core = lax.axis_size("core")
    images = latents[0]
    side_cells = images.shape[1]
    cell_count = images.shape[0] * side_cells * side_cells
    cols_out = cotangent.shape[4]

    activation = jax.nn.silu(images.astype(jnp.float32)).astype(jnp.bfloat16)
    kernel_all = lax.all_gather(weights[0].astype(jnp.bfloat16), DP_AXES, axis=0, tiled=True)
    padded_act = jnp.pad(activation, ((0, 0), (1, 1), (1, 1), (0, 0)))

    state = jnp.stack([weights[0], first_moment[0], second_moment[0]])
    state, kernel_all = lax.optimization_barrier((state, kernel_all))
    held_state = to_holders(state)
    summed = jnp.zeros((cell_count, cols_out), jnp.float32)
    for tap_index in range(9):
        summed = summed + jnp.dot(
            shifted(padded_act, tap_index, side_cells, False),
            kernel_all[:, tap_index * cols_out : (tap_index + 1) * cols_out],
            preferred_element_type=jnp.float32,
        )
    hidden = scale * summed
    deltas = (
        cotangent[0].reshape(cell_count, cols_out).astype(jnp.float32) * silu_slope(hidden)
    ).astype(jnp.bfloat16)
    moved_state = from_holders(held_state, sources)
    deltas_img = deltas.reshape(cotangent[0].shape)

    firsts = []
    for group in TAP_GROUPS:
        part = weight_rows(padded_act, deltas, group, side_cells, scale)
        firsts.append(core_stage(part, n_xlo, n_y, n_core))

    padded_del = jnp.pad(deltas_img, ((0, 0), (1, 1), (1, 1), (0, 0)))
    padded_del, firsts, moved_state = lax.optimization_barrier((padded_del, firsts, moved_state))
    grad_groups = [ring_stages(first, n_y) for first in firsts]
    back = jnp.zeros((cell_count, images.shape[3]), jnp.float32)
    for tap_index in range(9):
        back = back + lax.dot_general(
            shifted(padded_del, tap_index, side_cells, True),
            kernel_all[:, tap_index * cols_out : (tap_index + 1) * cols_out],
            (((1,), (1,)), ((), ())),
            preferred_element_type=jnp.float32,
        )
    back = scale * back
    slope_in = silu_slope(images.reshape(cell_count, images.shape[3]).astype(jnp.float32))
    latent_grad = (back * slope_in).astype(jnp.bfloat16).reshape(latents.shape)

    gradient = jnp.concatenate(grad_groups, axis=1)
    moved_grad = from_holders(to_holders(gradient[None]), sources)[0]
    updated, first_new, second_new = adam_update(
        moved_state[0], moved_state[1], moved_state[2], moved_grad
    )
    return (latent_grad, updated[None], first_new[None], second_new[None])


def solution(mesh):
    sub_mesh = Mesh(
        mesh.devices.reshape(2, mesh.shape["member"] // 2, 2, mesh.shape["dp"] // 4, 2),
        MEMBER_AXES + DP_AXES,
    )
    big = P(MEMBER_AXES, DP_AXES, None, None, None)
    state = P(MEMBER_AXES, DP_AXES, None)
    in_specs = (big, big, state, state, state, P())
    out_specs = (big, state, state, state)
    return jax.shard_map(step_body, mesh=sub_mesh, in_specs=in_specs, out_specs=out_specs, check_vma=False)
```

```python
import jax
import jax.numpy as jnp
from jax import lax
from jax.sharding import Mesh
from jax.sharding import PartitionSpec as P


CH_IN = 640
ADAM_STEP = 10


BETA_ONE = 0.9
BETA_TWO = 0.99
RATE = 0.05
EPSILON = 1e-08

MEMBER_AXES = ("x_hi", "z")
DP_AXES = ("x_lo", "y", "core")
TAP_GROUPS = ((0, 1, 2), (3, 4, 5), (6, 7, 8))


def silu_slope(values):
    sig = jax.nn.sigmoid(values)
    return sig * (1.0 + values * (1.0 - sig))


def shifted(padded, tap_index, side_cells, flip):
    tap_row = tap_index // 3
    tap_col = tap_index % 3
    if flip:
        tap_row = 2 - tap_row
        tap_col = 2 - tap_col
    window = padded[:, tap_row : tap_row + side_cells, tap_col : tap_col + side_cells, :]
    return window.reshape(-1, padded.shape[3])


def adam_update(weights_now, first_now, second_now, gradient):
    first_new = BETA_ONE * first_now + (1.0 - BETA_ONE) * gradient
    second_new = BETA_TWO * second_now + (1.0 - BETA_TWO) * gradient * gradient
    first_fix = 1.0 - BETA_ONE**ADAM_STEP
    second_fix = 1.0 - BETA_TWO**ADAM_STEP
    updated = weights_now - RATE * (first_new / first_fix) / (
        jnp.sqrt(second_new / second_fix) + EPSILON
    )
    return (updated, first_new, second_new)


def to_holders(stacked):
    members = lax.axis_size(MEMBER_AXES)
    layers, rows, cols = stacked.shape
    shaped = stacked.reshape(layers, members, rows // members, cols).transpose(1, 0, 2, 3)
    shaped = shaped.reshape(members, -1, cols)
    return lax.all_to_all(shaped, MEMBER_AXES, split_axis=0, concat_axis=0, tiled=True)


def from_holders(held, sources, shape):
    members = held.shape[0]
    picked = jnp.stack(
        [lax.dynamic_index_in_dim(held, sources[k], axis=0, keepdims=False) for k in range(members)]
    )
    returned = lax.all_to_all(picked, MEMBER_AXES, split_axis=0, concat_axis=0, tiled=True)
    layers, rows, cols = shape
    returned = returned.reshape(members, layers, rows // members, cols).transpose(1, 0, 2, 3)
    return returned.reshape(shape)


def swap(value, axis):
    return lax.ppermute(value, axis, [(0, 1), (1, 0)])


def weight_rows(padded_sel, deltas, group, side_cells, scale):
    blocks = []
    for tap_index in group:
        blocks.append(
            lax.dot_general(
                shifted(padded_sel, tap_index, side_cells, False),
                deltas,
                (((0,), (0,)), ((), ())),
                preferred_element_type=jnp.float32,
            )
        )
    return (scale * jnp.concatenate(blocks, axis=1)).astype(jnp.bfloat16)


def core_stage(part, n_xlo, n_y, n_core):
    my_core = lax.axis_index("core")
    part = part.reshape(n_xlo, n_y, n_core, -1, part.shape[1])
    keep = lax.dynamic_index_in_dim(part, my_core, axis=2, keepdims=False)
    give = lax.dynamic_index_in_dim(part, 1 - my_core, axis=2, keepdims=False)
    return (keep.astype(jnp.float32) + swap(give, "core").astype(jnp.float32)).astype(
        jnp.bfloat16
    )


def square_halving(stage1, flip_a, flip_b, pairs_a, pairs_b):
    my_y = lax.axis_index("y")
    across_a = flip_a(my_y)
    across_b = flip_b(my_y)
    send_ids = (across_a, flip_a(across_b))
    keep_ids = (my_y, across_b)
    send = jnp.stack([lax.dynamic_index_in_dim(stage1, i, axis=1, keepdims=False) for i in send_ids], 1)
    keep = jnp.stack([lax.dynamic_index_in_dim(stage1, i, axis=1, keepdims=False) for i in keep_ids], 1)
    got = lax.ppermute(send, "y", pairs_a)
    half = (keep.astype(jnp.float32) + got.astype(jnp.float32)).astype(jnp.bfloat16)
    got = lax.ppermute(half[:, 1], "y", pairs_b)
    return half[:, 0].astype(jnp.float32) + got.astype(jnp.float32)


def ring_stages(stage1, n_y):
    my_x = lax.axis_index("x_lo")
    flip_one = lambda y: y + 1 - 2 * (y % 2)
    flip_two = lambda y: n_y - 1 - y
    pairs_one = [(i, flip_one(i)) for i in range(n_y)]
    pairs_two = [(i, flip_two(i)) for i in range(n_y)]
    cols = stage1.shape[-1] // 2
    total = jnp.concatenate(
        [
            square_halving(stage1[..., :cols], flip_one, flip_two, pairs_one, pairs_two),
            square_halving(stage1[..., cols:], flip_two, flip_one, pairs_two, pairs_one),
        ],
        axis=-1,
    )
    stage2 = total.astype(jnp.bfloat16)
    keep = lax.dynamic_index_in_dim(stage2, my_x, axis=0, keepdims=False)
    give = lax.dynamic_index_in_dim(stage2, 1 - my_x, axis=0, keepdims=False)
    return keep.astype(jnp.float32) + swap(give, "x_lo").astype(jnp.float32)


def step_body(latents, cotangent, weights, first_moment, second_moment, sources):
    scale = (9 * CH_IN) ** (-0.5)
    n_xlo = lax.axis_size("x_lo")
    n_y = lax.axis_size("y")
    n_core = lax.axis_size("core")
    images = latents[0]
    side_cells = images.shape[1]
    cell_count = images.shape[0] * side_cells * side_cells
    cols_out = cotangent.shape[4]

    activation = jax.nn.silu(images.astype(jnp.float32)).astype(jnp.bfloat16)
    kernel_all = lax.all_gather(weights[0].astype(jnp.bfloat16), DP_AXES, axis=0, tiled=True)
    padded_act = jnp.pad(activation, ((0, 0), (1, 1), (1, 1), (0, 0)))

    state = jnp.stack([weights[0], first_moment[0], second_moment[0]])
    state, kernel_all = lax.optimization_barrier((state, kernel_all))
    held_state = to_holders(state)
    summed = jnp.zeros((cell_count, cols_out), jnp.float32)
    for tap_index in range(9):
        summed = summed + jnp.dot(
            shifted(padded_act, tap_index, side_cells, False),
            kernel_all[:, tap_index * cols_out : (tap_index + 1) * cols_out],
            preferred_element_type=jnp.float32,
        )
    hidden = scale * summed
    deltas = (
        cotangent[0].reshape(cell_count, cols_out).astype(jnp.float32) * silu_slope(hidden)
    ).astype(jnp.bfloat16)
    held_state, deltas = lax.optimization_barrier((held_state, deltas))
    moved_state = from_holders(held_state, sources, state.shape)
    deltas_img = deltas.reshape(cotangent[0].shape)

    firsts = []
    for group in TAP_GROUPS:
        part = weight_rows(padded_act, deltas, group, side_cells, scale)
        firsts.append(core_stage(part, n_xlo, n_y, n_core))

    padded_del = jnp.pad(deltas_img, ((0, 0), (1, 1), (1, 1), (0, 0)))
    padded_del, firsts, moved_state = lax.optimization_barrier((padded_del, firsts, moved_state))
    grad_groups = [ring_stages(first, n_y) for first in firsts]
    back = jnp.zeros((cell_count, images.shape[3]), jnp.float32)
    for tap_index in range(9):
        back = back + lax.dot_general(
            shifted(padded_del, tap_index, side_cells, True),
            kernel_all[:, tap_index * cols_out : (tap_index + 1) * cols_out],
            (((1,), (1,)), ((), ())),
            preferred_element_type=jnp.float32,
        )
    back = scale * back
    slope_in = silu_slope(images.reshape(cell_count, images.shape[3]).astype(jnp.float32))
    latent_grad = (back * slope_in).astype(jnp.bfloat16).reshape(latents.shape)

    gradient = jnp.concatenate(grad_groups, axis=1)
    moved_grad = from_holders(to_holders(gradient[None]), sources, (1,) + gradient.shape)[0]
    updated, first_new, second_new = adam_update(
        moved_state[0], moved_state[1], moved_state[2], moved_grad
    )
    return (latent_grad, updated[None], first_new[None], second_new[None])


def solution(mesh):
    sub_mesh = Mesh(
        mesh.devices.reshape(2, mesh.shape["member"] // 2, 2, mesh.shape["dp"] // 4, 2),
        MEMBER_AXES + DP_AXES,
    )
    big = P(MEMBER_AXES, DP_AXES, None, None, None)
    state = P(MEMBER_AXES, DP_AXES, None)
    in_specs = (big, big, state, state, state, P())
    out_specs = (big, state, state, state)
    return jax.shard_map(step_body, mesh=sub_mesh, in_specs=in_specs, out_specs=out_specs, check_vma=False)
```

```python
import jax
import jax.numpy as jnp
from jax import lax
from jax.sharding import Mesh
from jax.sharding import PartitionSpec as P


CH_IN = 640
ADAM_STEP = 10


BETA_ONE = 0.9
BETA_TWO = 0.99
RATE = 0.05
EPSILON = 1e-08

MEMBER_AXES = ("x_hi", "z")
DP_AXES = ("x_lo", "y", "core")
TAP_GROUPS = ((0, 1, 2), (3, 4, 5), (6, 7, 8))


def silu_slope(values):
    sig = jax.nn.sigmoid(values)
    return sig * (1.0 + values * (1.0 - sig))


def shifted(padded, tap_index, side_cells, flip):
    tap_row = tap_index // 3
    tap_col = tap_index % 3
    if flip:
        tap_row = 2 - tap_row
        tap_col = 2 - tap_col
    window = padded[:, tap_row : tap_row + side_cells, tap_col : tap_col + side_cells, :]
    return window.reshape(-1, padded.shape[3])


def adam_update(weights_now, first_now, second_now, gradient):
    first_new = BETA_ONE * first_now + (1.0 - BETA_ONE) * gradient
    second_new = BETA_TWO * second_now + (1.0 - BETA_TWO) * gradient * gradient
    first_fix = 1.0 - BETA_ONE**ADAM_STEP
    second_fix = 1.0 - BETA_TWO**ADAM_STEP
    updated = weights_now - RATE * (first_new / first_fix) / (
        jnp.sqrt(second_new / second_fix) + EPSILON
    )
    return (updated, first_new, second_new)


def to_holders(stacked):
    members = lax.axis_size(MEMBER_AXES)
    layers, rows, cols = stacked.shape
    shaped = stacked.reshape(layers, members, rows // members, cols).transpose(1, 0, 2, 3)
    shaped = shaped.reshape(members, -1, cols)
    return lax.all_to_all(shaped, MEMBER_AXES, split_axis=0, concat_axis=0, tiled=True)


def from_holders(held, sources, shape):
    members = held.shape[0]
    picked = jnp.stack(
        [lax.dynamic_index_in_dim(held, sources[k], axis=0, keepdims=False) for k in range(members)]
    )
    returned = lax.all_to_all(picked, MEMBER_AXES, split_axis=0, concat_axis=0, tiled=True)
    layers, rows, cols = shape
    returned = returned.reshape(members, layers, rows // members, cols).transpose(1, 0, 2, 3)
    return returned.reshape(shape)


def grad_to_holders(stacked):
    members = lax.axis_size(MEMBER_AXES)
    layers = stacked.shape[0]
    shaped = stacked.reshape(layers, members, stacked.shape[1] // members, stacked.shape[2])
    return lax.all_to_all(shaped, MEMBER_AXES, split_axis=1, concat_axis=1, tiled=True)


def grad_from_holders(held, sources):
    picked = jnp.stack(
        [lax.dynamic_index_in_dim(held, sources[k], axis=1, keepdims=False) for k in range(held.shape[1])],
        axis=1,
    )
    returned = lax.all_to_all(picked, MEMBER_AXES, split_axis=1, concat_axis=1, tiled=True)
    return returned.reshape(returned.shape[0], -1, returned.shape[3])


def swap(value, axis):
    return lax.ppermute(value, axis, [(0, 1), (1, 0)])


def weight_rows(padded_sel, deltas, group, side_cells, scale):
    blocks = []
    for tap_index in group:
        blocks.append(
            lax.dot_general(
                shifted(padded_sel, tap_index, side_cells, False),
                deltas,
                (((0,), (0,)), ((), ())),
                preferred_element_type=jnp.float32,
            )
        )
    return (scale * jnp.concatenate(blocks, axis=1)).astype(jnp.bfloat16)


def core_stage(part, n_xlo, n_y, n_core):
    my_core = lax.axis_index("core")
    part = part.reshape(n_xlo, n_y, n_core, -1, part.shape[1])
    keep = lax.dynamic_index_in_dim(part, my_core, axis=2, keepdims=False)
    give = lax.dynamic_index_in_dim(part, 1 - my_core, axis=2, keepdims=False)
    return (keep.astype(jnp.float32) + swap(give, "core").astype(jnp.float32)).astype(
        jnp.bfloat16
    )


def square_halving(stage1, flip_a, flip_b, pairs_a, pairs_b):
    my_y = lax.axis_index("y")
    across_a = flip_a(my_y)
    across_b = flip_b(my_y)
    send_ids = (across_a, flip_a(across_b))
    keep_ids = (my_y, across_b)
    send = jnp.stack([lax.dynamic_index_in_dim(stage1, i, axis=1, keepdims=False) for i in send_ids], 1)
    keep = jnp.stack([lax.dynamic_index_in_dim(stage1, i, axis=1, keepdims=False) for i in keep_ids], 1)
    got = lax.ppermute(send, "y", pairs_a)
    half = (keep.astype(jnp.float32) + got.astype(jnp.float32)).astype(jnp.bfloat16)
    got = lax.ppermute(half[:, 1], "y", pairs_b)
    return half[:, 0].astype(jnp.float32) + got.astype(jnp.float32)


def ring_stages(stage1, n_y):
    my_x = lax.axis_index("x_lo")
    flip_one = lambda y: y + 1 - 2 * (y % 2)
    flip_two = lambda y: n_y - 1 - y
    pairs_one = [(i, flip_one(i)) for i in range(n_y)]
    pairs_two = [(i, flip_two(i)) for i in range(n_y)]
    cols = stage1.shape[-1] // 2
    total = jnp.concatenate(
        [
            square_halving(stage1[..., :cols], flip_one, flip_two, pairs_one, pairs_two),
            square_halving(stage1[..., cols:], flip_two, flip_one, pairs_two, pairs_one),
        ],
        axis=-1,
    )
    stage2 = total.astype(jnp.bfloat16)
    keep = lax.dynamic_index_in_dim(stage2, my_x, axis=0, keepdims=False)
    give = lax.dynamic_index_in_dim(stage2, 1 - my_x, axis=0, keepdims=False)
    return keep.astype(jnp.float32) + swap(give, "x_lo").astype(jnp.float32)


def step_body(latents, cotangent, weights, first_moment, second_moment, sources):
    scale = (9 * CH_IN) ** (-0.5)
    n_xlo = lax.axis_size("x_lo")
    n_y = lax.axis_size("y")
    n_core = lax.axis_size("core")
    images = latents[0]
    side_cells = images.shape[1]
    cell_count = images.shape[0] * side_cells * side_cells
    cols_out = cotangent.shape[4]

    activation = jax.nn.silu(images.astype(jnp.float32)).astype(jnp.bfloat16)
    kernel_all = lax.all_gather(weights[0].astype(jnp.bfloat16), DP_AXES, axis=0, tiled=True)
    padded_act = jnp.pad(activation, ((0, 0), (1, 1), (1, 1), (0, 0)))

    state = jnp.stack([weights[0], first_moment[0], second_moment[0]])
    state, kernel_all = lax.optimization_barrier((state, kernel_all))
    held_state = to_holders(state)
    summed = jnp.zeros((cell_count, cols_out), jnp.float32)
    for tap_index in range(9):
        summed = summed + jnp.dot(
            shifted(padded_act, tap_index, side_cells, False),
            kernel_all[:, tap_index * cols_out : (tap_index + 1) * cols_out],
            preferred_element_type=jnp.float32,
        )
    hidden = scale * summed
    deltas = (
        cotangent[0].reshape(cell_count, cols_out).astype(jnp.float32) * silu_slope(hidden)
    ).astype(jnp.bfloat16)
    moved_state = from_holders(held_state, sources, state.shape)
    deltas_img = deltas.reshape(cotangent[0].shape)

    firsts = []
    for group in TAP_GROUPS:
        part = weight_rows(padded_act, deltas, group, side_cells, scale)
        firsts.append(core_stage(part, n_xlo, n_y, n_core))

    padded_del = jnp.pad(deltas_img, ((0, 0), (1, 1), (1, 1), (0, 0)))
    padded_del, firsts, moved_state = lax.optimization_barrier((padded_del, firsts, moved_state))
    grad_groups = [ring_stages(first, n_y) for first in firsts]
    back = jnp.zeros((cell_count, images.shape[3]), jnp.float32)
    for tap_index in range(9):
        back = back + lax.dot_general(
            shifted(padded_del, tap_index, side_cells, True),
            kernel_all[:, tap_index * cols_out : (tap_index + 1) * cols_out],
            (((1,), (1,)), ((), ())),
            preferred_element_type=jnp.float32,
        )
    back = scale * back
    slope_in = silu_slope(images.reshape(cell_count, images.shape[3]).astype(jnp.float32))
    latent_grad = (back * slope_in).astype(jnp.bfloat16).reshape(latents.shape)

    gradient = jnp.concatenate(grad_groups, axis=1)
    moved_grad = grad_from_holders(grad_to_holders(gradient[None]), sources)[0]
    updated, first_new, second_new = adam_update(
        moved_state[0], moved_state[1], moved_state[2], moved_grad
    )
    return (latent_grad, updated[None], first_new[None], second_new[None])


def solution(mesh):
    sub_mesh = Mesh(
        mesh.devices.reshape(2, mesh.shape["member"] // 2, 2, mesh.shape["dp"] // 4, 2),
        MEMBER_AXES + DP_AXES,
    )
    big = P(MEMBER_AXES, DP_AXES, None, None, None)
    state = P(MEMBER_AXES, DP_AXES, None)
    in_specs = (big, big, state, state, state, P())
    out_specs = (big, state, state, state)
    return jax.shard_map(step_body, mesh=sub_mesh, in_specs=in_specs, out_specs=out_specs, check_vma=False)
```

```python
import jax
import jax.numpy as jnp
from jax import lax
from jax.sharding import Mesh
from jax.sharding import PartitionSpec as P


CH_IN = 640
ADAM_STEP = 10


BETA_ONE = 0.9
BETA_TWO = 0.99
RATE = 0.05
EPSILON = 1e-08

MEMBER_AXES = ("x_hi", "z")
DP_AXES = ("x_lo", "y", "core")
TAP_GROUPS = ((0, 1, 2), (3, 4, 5), (6, 7, 8))


def silu_slope(values):
    sig = jax.nn.sigmoid(values)
    return sig * (1.0 + values * (1.0 - sig))


def shifted(padded, tap_index, side_cells, flip):
    tap_row = tap_index // 3
    tap_col = tap_index % 3
    if flip:
        tap_row = 2 - tap_row
        tap_col = 2 - tap_col
    window = padded[:, tap_row : tap_row + side_cells, tap_col : tap_col + side_cells, :]
    return window.reshape(-1, padded.shape[3])


def adam_update(weights_now, first_now, second_now, gradient):
    first_new = BETA_ONE * first_now + (1.0 - BETA_ONE) * gradient
    second_new = BETA_TWO * second_now + (1.0 - BETA_TWO) * gradient * gradient
    first_fix = 1.0 - BETA_ONE**ADAM_STEP
    second_fix = 1.0 - BETA_TWO**ADAM_STEP
    updated = weights_now - RATE * (first_new / first_fix) / (
        jnp.sqrt(second_new / second_fix) + EPSILON
    )
    return (updated, first_new, second_new)


def member_leading(stacked):
    members = lax.axis_size(MEMBER_AXES)
    layers, rows, cols = stacked.shape
    shaped = stacked.reshape(layers, members, rows // members, cols).transpose(1, 0, 2, 3)
    return shaped.reshape(members, -1, cols)


def to_holders(shaped):
    return lax.all_to_all(shaped, MEMBER_AXES, split_axis=0, concat_axis=0, tiled=True)


def from_holders(held, sources, shape):
    members = held.shape[0]
    picked = jnp.stack(
        [lax.dynamic_index_in_dim(held, sources[k], axis=0, keepdims=False) for k in range(members)]
    )
    returned = lax.all_to_all(picked, MEMBER_AXES, split_axis=0, concat_axis=0, tiled=True)
    layers, rows, cols = shape
    returned = returned.reshape(members, layers, rows // members, cols).transpose(1, 0, 2, 3)
    return returned.reshape(shape)


def grad_to_holders(stacked):
    members = lax.axis_size(MEMBER_AXES)
    layers = stacked.shape[0]
    shaped = stacked.reshape(layers, members, stacked.shape[1] // members, stacked.shape[2])
    return lax.all_to_all(shaped, MEMBER_AXES, split_axis=1, concat_axis=1, tiled=True)


def grad_from_holders(held, sources):
    picked = jnp.stack(
        [lax.dynamic_index_in_dim(held, sources[k], axis=1, keepdims=False) for k in range(held.shape[1])],
        axis=1,
    )
    returned = lax.all_to_all(picked, MEMBER_AXES, split_axis=1, concat_axis=1, tiled=True)
    return returned.reshape(returned.shape[0], -1, returned.shape[3])


def swap(value, axis):
    return lax.ppermute(value, axis, [(0, 1), (1, 0)])


def weight_rows(padded_sel, deltas, group, side_cells, scale):
    blocks = []
    for tap_index in group:
        blocks.append(
            lax.dot_general(
                shifted(padded_sel, tap_index, side_cells, False),
                deltas,
                (((0,), (0,)), ((), ())),
                preferred_element_type=jnp.float32,
            )
        )
    return (scale * jnp.concatenate(blocks, axis=1)).astype(jnp.bfloat16)


def core_stage(part, n_xlo, n_y, n_core):
    my_core = lax.axis_index("core")
    part = part.reshape(n_xlo, n_y, n_core, -1, part.shape[1])
    keep = lax.dynamic_index_in_dim(part, my_core, axis=2, keepdims=False)
    give = lax.dynamic_index_in_dim(part, 1 - my_core, axis=2, keepdims=False)
    return (keep.astype(jnp.float32) + swap(give, "core").astype(jnp.float32)).astype(
        jnp.bfloat16
    )


def square_halving(stage1, flip_a, flip_b, pairs_a, pairs_b):
    my_y = lax.axis_index("y")
    across_a = flip_a(my_y)
    across_b = flip_b(my_y)
    send_ids = (across_a, flip_a(across_b))
    keep_ids = (my_y, across_b)
    send = jnp.stack([lax.dynamic_index_in_dim(stage1, i, axis=1, keepdims=False) for i in send_ids], 1)
    keep = jnp.stack([lax.dynamic_index_in_dim(stage1, i, axis=1, keepdims=False) for i in keep_ids], 1)
    got = lax.ppermute(send, "y", pairs_a)
    half = (keep.astype(jnp.float32) + got.astype(jnp.float32)).astype(jnp.bfloat16)
    got = lax.ppermute(half[:, 1], "y", pairs_b)
    return half[:, 0].astype(jnp.float32) + got.astype(jnp.float32)


def ring_stages(stage1, n_y):
    my_x = lax.axis_index("x_lo")
    flip_one = lambda y: y + 1 - 2 * (y % 2)
    flip_two = lambda y: n_y - 1 - y
    pairs_one = [(i, flip_one(i)) for i in range(n_y)]
    pairs_two = [(i, flip_two(i)) for i in range(n_y)]
    cols = stage1.shape[-1] // 2
    total = jnp.concatenate(
        [
            square_halving(stage1[..., :cols], flip_one, flip_two, pairs_one, pairs_two),
            square_halving(stage1[..., cols:], flip_two, flip_one, pairs_two, pairs_one),
        ],
        axis=-1,
    )
    stage2 = total.astype(jnp.bfloat16)
    keep = lax.dynamic_index_in_dim(stage2, my_x, axis=0, keepdims=False)
    give = lax.dynamic_index_in_dim(stage2, 1 - my_x, axis=0, keepdims=False)
    return keep.astype(jnp.float32) + swap(give, "x_lo").astype(jnp.float32)


def step_body(latents, cotangent, weights, first_moment, second_moment, sources):
    scale = (9 * CH_IN) ** (-0.5)
    n_xlo = lax.axis_size("x_lo")
    n_y = lax.axis_size("y")
    n_core = lax.axis_size("core")
    images = latents[0]
    side_cells = images.shape[1]
    cell_count = images.shape[0] * side_cells * side_cells
    cols_out = cotangent.shape[4]

    activation = jax.nn.silu(images.astype(jnp.float32)).astype(jnp.bfloat16)
    kernel_all = lax.all_gather(weights[0].astype(jnp.bfloat16), DP_AXES, axis=0, tiled=True)
    padded_act = jnp.pad(activation, ((0, 0), (1, 1), (1, 1), (0, 0)))

    state = jnp.stack([weights[0], first_moment[0], second_moment[0]])
    shaped_state, kernel_all = lax.optimization_barrier((member_leading(state), kernel_all))
    held_state = to_holders(shaped_state)
    summed = jnp.zeros((cell_count, cols_out), jnp.float32)
    for tap_index in range(9):
        summed = summed + jnp.dot(
            shifted(padded_act, tap_index, side_cells, False),
            kernel_all[:, tap_index * cols_out : (tap_index + 1) * cols_out],
            preferred_element_type=jnp.float32,
        )
    hidden = scale * summed
    deltas = (
        cotangent[0].reshape(cell_count, cols_out).astype(jnp.float32) * silu_slope(hidden)
    ).astype(jnp.bfloat16)
    held_state, deltas = lax.optimization_barrier((held_state, deltas))
    moved_state = from_holders(held_state, sources, state.shape)
    deltas_img = deltas.reshape(cotangent[0].shape)

    firsts = []
    for group in TAP_GROUPS:
        part = weight_rows(padded_act, deltas, group, side_cells, scale)
        firsts.append(core_stage(part, n_xlo, n_y, n_core))

    padded_del = jnp.pad(deltas_img, ((0, 0), (1, 1), (1, 1), (0, 0)))
    padded_del, firsts, moved_state = lax.optimization_barrier((padded_del, firsts, moved_state))
    grad_groups = [ring_stages(first, n_y) for first in firsts]
    back = jnp.zeros((cell_count, images.shape[3]), jnp.float32)
    for tap_index in range(9):
        back = back + lax.dot_general(
            shifted(padded_del, tap_index, side_cells, True),
            kernel_all[:, tap_index * cols_out : (tap_index + 1) * cols_out],
            (((1,), (1,)), ((), ())),
            preferred_element_type=jnp.float32,
        )
    back = scale * back
    slope_in = silu_slope(images.reshape(cell_count, images.shape[3]).astype(jnp.float32))
    latent_grad = (back * slope_in).astype(jnp.bfloat16).reshape(latents.shape)

    gradient = jnp.concatenate(grad_groups, axis=1)
    moved_grad = grad_from_holders(grad_to_holders(gradient[None]), sources)[0]
    updated, first_new, second_new = adam_update(
        moved_state[0], moved_state[1], moved_state[2], moved_grad
    )
    return (latent_grad, updated[None], first_new[None], second_new[None])


def solution(mesh):
    sub_mesh = Mesh(
        mesh.devices.reshape(2, mesh.shape["member"] // 2, 2, mesh.shape["dp"] // 4, 2),
        MEMBER_AXES + DP_AXES,
    )
    big = P(MEMBER_AXES, DP_AXES, None, None, None)
    state = P(MEMBER_AXES, DP_AXES, None)
    in_specs = (big, big, state, state, state, P())
    out_specs = (big, state, state, state)
    return jax.shard_map(step_body, mesh=sub_mesh, in_specs=in_specs, out_specs=out_specs, check_vma=False)
```
